128 devices in a mesh: req: 16 (over y, z_hi, core), kv: 8 (over z_lo, x).
Axes of the slice: x: 4, y: 4, z: 4 (z_hi: 2, z_lo: 2; z = z_hi * 2 + z_lo), core: 2. Of those that a mesh axis runs over, the one named last changes fastest.
Arguments:
- tokens: bfloat16 [1024, 8192], P(None, 'req'), may hold values from -40 to 40
- norm_in: bfloat16 [8192], P('req'), may hold values from 0.099609375 to 1.8984375
- w_qkv: bfloat16 [8192, 10240], P('req', 'kv'), may hold values from -0.0625 to 0.0625
- qkv_bias: bfloat16 [10240], P('kv'), may hold values from -12 to 12
- w_out: bfloat16 [8192, 8192], P('kv', 'req'), may hold values from -0.0625 to 0.0625
- norm_mid: bfloat16 [8192], P('req'), may hold values from 0.099609375 to 1.8984375
- w_gate: bfloat16 [8192, 29568], P('req', 'kv'), may hold values from -0.0625 to 0.0625
- w_up: bfloat16 [8192, 29568], P('req', 'kv'), may hold values from -0.0625 to 0.0625
- w_down: bfloat16 [29568, 8192], P('kv', 'req'), may hold values from -0.03125 to 0.03125
- short_keys: bfloat16 [1024, 256, 8, 128], P('req', None, 'kv'), may hold values from -310 to 310
- short_values: bfloat16 [1024, 256, 8, 128], P('req', None, 'kv'), may hold values from -6 to 6
- short_len: int32 [1024], P('req'), may hold values from 1 to 256, 131072 in all
- long_keys: bfloat16 [16, 8192, 8, 128], P('req', None, 'kv'), may hold values from -310 to 310
- long_values: bfloat16 [16, 8192, 8, 128], P('req', None, 'kv'), may hold values from -6 to 6
- long_len: int32 [16], replicated, may hold values from 0 to 8192, as said below
- positions: int32 [1024], P('req'), may hold values from 0 to 32767
Outputs:
- layer_out: bfloat16 [1024, 8192], P(None, 'req')
The draws below stay inside these ranges and needn't reach their ends.
Inputs may be any that keep to these rules, and one draw needn't show every extreme that they name: `short_len`: short lengths sum to 131072 and the largest is 256. `long_len`: exactly 8 segments are live, the others have length 0; live ones hold at least 4096 slots and one holds 8192.
All inputs are finite; a program needn't handle non-finite values. No bound on the sum of `short_len` on one device may be relied on, other than what follows from the above.
Results may differ from the reference program's by a relative error of at most 0.0085.
Values may be sent and summed in bfloat16 or wider, within the bound.
No kernel may reach another device: no remote copies, remote signals or barrier semaphores. Data moves between devices by JAX's collectives and lax.ppermute only.
A program may use at most 128 MiB of HBM per device.

```python
import math
import jax
import jax.numpy as jnp
import numpy as np
from jax import lax

D = 8192
FF = 29568
HQ = 64
KVH = 8
HD = 128
SHORT_CAP = 256
LONG_CAP = 8192
REQ_DEV = 64
GROUP = 8
REQUESTS = 1024
SLOTS = 16
N_REQ = 16


def draw_tokens(key, part):
    first, second, third = jax.random.split(key, 3)
    place = jnp.arange(D, dtype=jnp.float32)[None, :] / (D - 1)
    base = jnp.clip(jax.random.normal(first, (REQUESTS, D), jnp.float32), -6.0, 6.0)
    rows = jnp.exp(jax.random.uniform(second, (REQUESTS, 1), jnp.float32, math.log(0.3), math.log(3.0)))
    rough = jnp.exp(jax.random.uniform(third, (1, D), jnp.float32, math.log(0.7), math.log(1.4)))
    columns = rough * jnp.exp(math.log(3.0) * place)
    return jnp.clip(base * rows * columns, -40.0, 40.0).astype(jnp.bfloat16)


def draw_qkv_bias(key, part):
    values = jnp.clip(0.5 * jax.random.normal(key, (KVH, GROUP + 2, HD), jnp.float32), -3.0, 3.0)
    return values.reshape(KVH * (GROUP + 2) * HD).astype(jnp.bfloat16)


def spiked_keys(key, count, length):
    first = jax.random.fold_in(jax.random.fold_in(key, 7), 0)
    shape = (count, length, KVH, HD)
    values = jnp.clip(jax.random.normal(first, shape, jnp.float32), -6.0, 6.0)
    return values.astype(jnp.bfloat16)


def draw_short_keys(key, part):
    return spiked_keys(key, REQUESTS, SHORT_CAP)


def draw_long_keys(key, part):
    return spiked_keys(key, SLOTS, LONG_CAP)


def draw_long_len(key, part):
    first, second = jax.random.split(jax.random.fold_in(key, 11))
    order = jax.random.permutation(first, SLOTS)
    sizes = jax.random.randint(second, (SLOTS,), LONG_CAP // 2, LONG_CAP + 1)
    sizes = jnp.where(order == 0, LONG_CAP, sizes)
    return jnp.where(order < SLOTS // 2, sizes, 0).astype(jnp.int32)


def place_ends(values, own_key, low, high):
    longest = values.shape.index(max(values.shape))
    spots = []
    for shift in (0, 1):
        where = [jax.random.randint(jax.random.fold_in(own_key, axis), (), 0, length) for axis, length in enumerate(values.shape)]
        where[longest] = (where[longest] + shift) % values.shape[longest]
        spots.append(tuple(where))
    return values.at[spots[0]].set(low).at[spots[1]].set(high)


def block_scale(key, shape, cuts, least, largest):
    factor_of = 1.0
    for position, shards_of in cuts:
        steps = jax.random.uniform(jax.random.fold_in(jax.random.fold_in(key, 6), position), (shards_of,), jnp.float32, least / len(cuts), largest / len(cuts))
        factor_of = factor_of * jnp.repeat(jnp.exp(steps), shape[position] // shards_of).reshape((-1,) + (1,) * (len(shape) - 1 - position))
    return factor_of


def profile(number_of, total, reach, slope):
    loads = [(1 << 20) // math.isqrt(standing ** slope) + 1 for standing in range(2, number_of + 1)]
    surplus, counts = total - reach - (number_of - 1), [1] * (number_of - 1)
    while surplus > 0:
        free = [i for i in range(number_of - 1) if counts[i] < reach]
        pool, remaining = sum([loads[i] for i in free]), surplus
        for i in free:
            more = min(reach - counts[i], max(1, remaining * loads[i] // pool), surplus)
            counts[i] = counts[i] + more
            surplus = surplus - more
    return np.array([reach] + counts)


def ragged(key, count, total, bound, skew):
    if count == 2:
        one = jax.random.randint(key, (), max(1, total - bound), min(bound, total - 1) + 1)
        return jnp.stack([one, total - one])
    lengths = jnp.asarray(profile(count, total, bound, skew), jnp.int32)
    couples = (count - 1) // 2
    donor, receiver = lengths[1:1 + 2 * couples:2], lengths[2:2 + 2 * couples:2]
    room = jnp.minimum(donor - 1, bound - receiver)
    passed = jax.random.randint(jax.random.fold_in(key, 1), (couples,), 0, 1 << 20) % (room + 1)
    lengths = lengths.at[1:1 + 2 * couples:2].set(donor - passed).at[2:2 + 2 * couples:2].set(receiver + passed)
    return lengths[jax.random.permutation(jax.random.fold_in(key, 2), count)]


def normal_values(key, shape, scale, reach, shards=(), held_as=jnp.bfloat16):
    values = jax.random.normal(key, shape, jnp.float32) * scale
    if len(shards) > 0:
        values = block_scale(key, shape, shards, -0.22, 0.18) * values
    return jnp.clip(values, min=-reach, max=reach).astype(held_as)


def setup_inputs(seed: int = 0) -> dict:
    splits = jax.random.split(jax.random.key(seed), 17)
    return {
        "tokens": draw_tokens(jax.random.fold_in(splits[16], 71), 0),
        "norm_in": jnp.clip(1.0 + 0.18 * jax.random.normal(splits[1], (D,), jnp.float32), 0.099609375, 1.8984375).astype(jnp.bfloat16),
        "w_qkv": normal_values(splits[2], (D, KVH * (GROUP + 2) * HD), D ** -0.5, 0.0625, ((0, 16), (1, 8))),
        "qkv_bias": draw_qkv_bias(jax.random.fold_in(splits[16], 71), 0),
        "w_out": normal_values(splits[4], (HQ * HD, D), (HQ * HD) ** -0.5, 0.0625, ((0, 8), (1, 16))),
        "norm_mid": jnp.clip(1.0 + 0.18 * jax.random.normal(splits[5], (D,), jnp.float32), 0.099609375, 1.8984375).astype(jnp.bfloat16),
        "w_gate": normal_values(splits[6], (D, FF), D ** -0.5, 0.0625, ((0, 16), (1, 8))),
        "w_up": normal_values(splits[7], (D, FF), D ** -0.5, 0.0625, ((0, 16), (1, 8))),
        "w_down": normal_values(splits[8], (FF, D), FF ** -0.5, 0.03125, ((0, 8), (1, 16))),
        "short_keys": draw_short_keys(jax.random.fold_in(splits[16], 71), 0),
        "short_values": normal_values(splits[10], (REQUESTS, SHORT_CAP, KVH, HD), 1.0, 6.0, ((0, 16), (2, 8))),
        "short_len": ragged(splits[11], REQUESTS, REQ_DEV * N_REQ * SHORT_CAP // 2, SHORT_CAP, 2).astype(jnp.int32),
        "long_keys": draw_long_keys(jax.random.fold_in(splits[16], 71), 0),
        "long_values": normal_values(splits[13], (SLOTS, LONG_CAP, KVH, HD), 1.0, 6.0, ((0, 16), (2, 8))),
        "long_len": draw_long_len(jax.random.fold_in(splits[16], 71), 0),
        "positions": place_ends(jax.random.randint(splits[15], (REQUESTS,), 0, 32768), jax.random.fold_in(splits[15], 1), 0, 32767).astype(jnp.int32),
    }


EPS = 1e-06
THETA = 1000000.0
NEGATIVE = -1e+30

def rms_norm(hidden, gain):
    wide = hidden.astype(jnp.float32)
    square_sum = lax.optimization_barrier(jnp.sum(wide * wide, axis=1, keepdims=True))
    return (wide * lax.rsqrt(square_sum / D + EPS) * gain.astype(jnp.float32)[None, :]).astype(jnp.bfloat16)

def rotate(values, angles):
    half = values.shape[-1] // 2
    first = values[..., :half]
    second = values[..., half:]
    cosine = jnp.cos(angles)
    sine = jnp.sin(angles)
    return jnp.concatenate([first * cosine - second * sine, second * cosine + first * sine], axis=-1)

def widen(values):
    return lax.optimization_barrier(values.astype(jnp.bfloat16)).astype(jnp.float32)

def block_sum(left, right):
    width = D // N_REQ

    def step(carry, index):
        start = (index * width).astype(jnp.int32)
        part_left = lax.dynamic_slice_in_dim(left, start, width, 1)
        part_right = lax.dynamic_slice_in_dim(right, start, width, 0)
        return (carry + widen(jnp.dot(part_left, part_right, preferred_element_type=jnp.float32)), None)
    init = jnp.zeros((left.shape[0], right.shape[1]), jnp.float32)
    return lax.scan(step, init, jnp.arange(N_REQ, dtype=jnp.int32))[0]

def reference(tokens, norm_in, w_qkv, qkv_bias, w_out, norm_mid, w_gate, w_up, w_down, short_keys, short_values, short_len, long_keys, long_values, long_len, positions):
    scale = HD ** (-0.5)
    normed = rms_norm(tokens, norm_in)
    united = block_sum(normed, w_qkv) + qkv_bias.astype(jnp.float32)[None, :]
    united = united.reshape(REQUESTS, KVH, GROUP + 2, HD)
    inv_freq = THETA ** (-(2.0 * jnp.arange(HD // 2, dtype=jnp.float32)) / HD)
    angles = positions.astype(jnp.float32)[:, None] * inv_freq[None, :]
    queries = widen(rotate(united[:, :, :GROUP], angles[:, None, None, :]))
    new_keys = widen(rotate(united[:, :, GROUP], angles[:, None, :]))
    new_values = widen(united[:, :, GROUP + 1])
    short_raw = jnp.einsum('rhgd,rshd->rhgs', queries, short_keys.astype(jnp.float32)) * scale
    live = jnp.arange(SHORT_CAP)[None, :] < short_len[:, None]
    short_raw = jnp.where(live[:, None, None, :], short_raw, NEGATIVE)
    own_raw = jnp.einsum('rhgd,rhd->rhg', queries, new_keys) * scale
    owner_queries = queries.reshape(SLOTS, REQ_DEV, KVH, GROUP, HD)[:, 0]

    def long_score(items):
        query, keys, length = items
        raw = jnp.einsum('hgd,lhd->hgl', query, keys.astype(jnp.float32)) * scale
        long_live = jnp.arange(LONG_CAP) < length
        return jnp.where(long_live[None, None, :], raw, NEGATIVE)
    long_raw = lax.map(long_score, (owner_queries, long_keys, long_len))
    peak = jnp.maximum(lax.optimization_barrier(jnp.max(short_raw, axis=3)), own_raw).reshape(SLOTS, REQ_DEV, KVH, GROUP)
    owner_peak = jnp.maximum(peak[:, 0], lax.optimization_barrier(jnp.max(long_raw, axis=3)))
    peak = peak.at[:, 0].set(owner_peak).reshape(REQUESTS, KVH, GROUP)
    short_weights = jnp.exp(short_raw - peak[..., None])
    own_weights = jnp.exp(own_raw - peak)
    total = lax.optimization_barrier(jnp.sum(short_weights, axis=3)) + own_weights
    summed = jnp.einsum('rhgs,rshd->rhgd', widen(short_weights), short_values.astype(jnp.float32))
    summed = summed + widen(own_weights)[..., None] * new_values[:, :, None, :]

    def long_sum(items):
        raw, values, highest = items
        weights = jnp.exp(raw - highest[:, :, None])
        return (lax.optimization_barrier(jnp.sum(weights, axis=2)), jnp.einsum('hgl,lhd->hgd', widen(weights), values.astype(jnp.float32)))
    long_total, long_summed = lax.map(long_sum, (long_raw, long_values, owner_peak))
    total = total.reshape(SLOTS, REQ_DEV, KVH, GROUP).at[:, 0].add(long_total).reshape(REQUESTS, KVH, GROUP)
    summed = summed.reshape(SLOTS, REQ_DEV, KVH, GROUP, HD).at[:, 0].add(long_summed).reshape(REQUESTS, KVH, GROUP, HD)
    attended = (summed / total[..., None]).astype(jnp.bfloat16).reshape(REQUESTS, HQ * HD)
    projected = jnp.dot(attended, w_out, preferred_element_type=jnp.float32)
    residual = lax.optimization_barrier((tokens.astype(jnp.float32) + projected).astype(jnp.bfloat16))
    mixed_in = rms_norm(residual, norm_mid)
    gate = block_sum(mixed_in, w_gate)
    up = block_sum(mixed_in, w_up)
    act = (jax.nn.silu(gate) * up).astype(jnp.bfloat16)
    down = jnp.dot(act, w_down, preferred_element_type=jnp.float32)
    return (residual.astype(jnp.float32) + down).astype(jnp.bfloat16)
```

```python
import jax
import jax.numpy as jnp
from jax import lax
from jax.sharding import PartitionSpec as P

D = 8192
HD = 128
SHORT_CAP = 256
LONG_CAP = 8192
REQ_DEV = 64
GROUP = 8


EPS = 1e-06
THETA = 1000000.0
NEGATIVE = -1e30


def rotate(values, angles):
    half = values.shape[-1] // 2
    first = values[..., :half]
    second = values[..., half:]
    cosine = jnp.cos(angles)
    sine = jnp.sin(angles)
    return jnp.concatenate(
        [first * cosine - second * sine, second * cosine + first * sine], axis=-1
    )


def weigh(short_raw, own_raw, short_values, own_values, peak):
    short_weights = jnp.exp(short_raw - peak[..., None])
    own_weights = jnp.exp(own_raw - peak)
    total = jnp.sum(short_weights, axis=3) + own_weights
    summed = jnp.einsum(
        "rhgs,rshd->rhgd",
        short_weights.astype(jnp.bfloat16),
        short_values,
        preferred_element_type=jnp.float32,
    )
    summed = summed + jnp.einsum(
        "rhg,rhd->rhgd",
        own_weights.astype(jnp.bfloat16),
        own_values,
        preferred_element_type=jnp.float32,
    )
    return (total, summed)


def per_device(
    tokens,
    norm_in,
    w_qkv,
    qkv_bias,
    w_out,
    norm_mid,
    w_gate,
    w_up,
    w_down,
    short_keys,
    short_values,
    short_len,
    long_keys,
    long_values,
    long_len,
    positions,
):
    heads_here = short_keys.shape[2]
    scale = HD ** (-0.5)
    wide = tokens.astype(jnp.float32)
    slot = lax.axis_index("req")
    square_in = lax.psum(jnp.sum(wide * wide, axis=1), "req")
    gained = (wide * norm_in.astype(jnp.float32)[None, :]).astype(jnp.bfloat16)
    united = lax.psum_scatter(
        jnp.dot(gained, w_qkv, preferred_element_type=jnp.float32).astype(jnp.bfloat16),
        "req",
        scatter_dimension=0,
        tiled=True,
    ).astype(jnp.float32)
    scale_in = lax.rsqrt(lax.dynamic_slice_in_dim(square_in, slot * REQ_DEV, REQ_DEV) / D + EPS)
    united = (united * scale_in[:, None] + qkv_bias.astype(jnp.float32)[None, :]).reshape(
        REQ_DEV, heads_here, GROUP + 2, HD
    )
    inv_freq = THETA ** (-(2.0 * jnp.arange(HD // 2, dtype=jnp.float32)) / HD)
    angles = positions.astype(jnp.float32)[:, None] * inv_freq[None, :]
    queries = rotate(united[:, :, :GROUP], angles[:, None, None, :]).astype(jnp.bfloat16)
    new_keys = rotate(united[:, :, GROUP], angles[:, None, :]).astype(jnp.bfloat16)
    new_values = united[:, :, GROUP + 1].astype(jnp.bfloat16)
    short_raw = (
        jnp.einsum("rhgd,rshd->rhgs", queries, short_keys, preferred_element_type=jnp.float32)
        * scale
    )
    live = jnp.arange(SHORT_CAP)[None, :] < short_len[:, None]
    short_raw = jnp.where(live[:, None, None, :], short_raw, NEGATIVE)
    own_raw = (
        jnp.einsum("rhgd,rhd->rhg", queries, new_keys, preferred_element_type=jnp.float32) * scale
    )
    peak = jnp.maximum(jnp.max(short_raw, axis=3), own_raw)
    slot_len = lax.dynamic_index_in_dim(long_len, slot, 0, keepdims=False)
    long_raw = (
        jnp.einsum("hgd,lhd->hgl", queries[0], long_keys[0], preferred_element_type=jnp.float32)
        * scale
    )
    long_live = jnp.arange(LONG_CAP) < slot_len
    long_raw = jnp.where(long_live[None, None, :], long_raw, NEGATIVE)
    first_peak = jnp.maximum(peak[0], jnp.max(long_raw, axis=2))
    peak = jnp.concatenate([first_peak[None], peak[1:]], axis=0)
    total, summed = weigh(short_raw, own_raw, short_values, new_values, peak)
    long_weights = jnp.where(
        long_live[None, None, :], jnp.exp(long_raw - first_peak[:, :, None]), 0.0
    )
    long_summed = jnp.einsum(
        "hgl,lhd->hgd",
        long_weights.astype(jnp.bfloat16),
        long_values[0],
        preferred_element_type=jnp.float32,
    )
    total = total.at[0].add(jnp.sum(long_weights, axis=2))
    summed = summed.at[0].add(long_summed)
    attended = (
        (summed / total[..., None]).astype(jnp.bfloat16).reshape(REQ_DEV, heads_here * GROUP * HD)
    )
    out_part = jnp.dot(
        lax.all_gather(attended, "req", axis=0, tiled=True),
        w_out,
        preferred_element_type=jnp.float32,
    )
    projected = lax.psum(out_part.astype(jnp.bfloat16), "kv").astype(jnp.float32)
    residual = lax.optimization_barrier((wide + projected).astype(jnp.bfloat16))
    resid_wide = residual.astype(jnp.float32)
    square_mid = lax.psum(jnp.sum(resid_wide * resid_wide, axis=1), "req")
    mixed_in = (resid_wide * norm_mid.astype(jnp.float32)[None, :]).astype(jnp.bfloat16)
    units = w_gate.shape[1]
    padded = -(-units // 128) * 128
    w_gate_up = jnp.concatenate(
        [
            jnp.pad(w_gate, ((0, 0), (0, padded - units))),
            jnp.pad(w_up, ((0, 0), (0, padded - units))),
        ],
        axis=1,
    )
    gate_up = lax.psum_scatter(
        jnp.dot(mixed_in, w_gate_up, preferred_element_type=jnp.float32).astype(jnp.bfloat16),
        "req",
        scatter_dimension=0,
        tiled=True,
    ).astype(jnp.float32)
    scale_mid = lax.rsqrt(lax.dynamic_slice_in_dim(square_mid, slot * REQ_DEV, REQ_DEV) / D + EPS)
    gate = gate_up[:, :units] * scale_mid[:, None]
    up = gate_up[:, padded : padded + units] * scale_mid[:, None]
    act = (jax.nn.silu(gate) * up).astype(jnp.bfloat16)
    down_part = jnp.dot(
        lax.all_gather(act, "req", axis=0, tiled=True), w_down, preferred_element_type=jnp.float32
    )
    down = lax.psum(down_part.astype(jnp.bfloat16), "kv").astype(jnp.float32)
    return (resid_wide + down).astype(jnp.bfloat16)


def solution(mesh):
    placed = (
        P(None, "req"),
        P("req"),
        P("req", "kv"),
        P("kv"),
        P("kv", "req"),
        P("req"),
        P("req", "kv"),
        P("req", "kv"),
        P("kv", "req"),
        P("req", None, "kv", None),
        P("req", None, "kv", None),
        P("req"),
        P("req", None, "kv", None),
        P("req", None, "kv", None),
        P(),
        P("req"),
    )
    return jax.shard_map(
        per_device, mesh=mesh, in_specs=placed, out_specs=P(None, "req"), check_vma=False
    )
```

```python
import jax
import jax.numpy as jnp
from jax import lax
from jax.sharding import PartitionSpec as P

D = 8192
HD = 128
SHORT_CAP = 256
LONG_CAP = 8192
REQ_DEV = 64
GROUP = 8


EPS = 1e-06
THETA = 1000000.0
NEGATIVE = -1e30


def rotate(values, angles):
    half = values.shape[-1] // 2
    first = values[..., :half]
    second = values[..., half:]
    cosine = jnp.cos(angles)
    sine = jnp.sin(angles)
    return jnp.concatenate(
        [first * cosine - second * sine, second * cosine + first * sine], axis=-1
    )


def weigh(short_raw, own_raw, short_values, own_values, peak):
    short_weights = jnp.exp(short_raw - peak[..., None])
    own_weights = jnp.exp(own_raw - peak)
    total = jnp.sum(short_weights, axis=3) + own_weights
    summed = jnp.einsum(
        "rhgs,rshd->rhgd",
        short_weights.astype(jnp.bfloat16),
        short_values,
        preferred_element_type=jnp.float32,
    )
    summed = summed + jnp.einsum(
        "rhg,rhd->rhgd",
        own_weights.astype(jnp.bfloat16),
        own_values,
        preferred_element_type=jnp.float32,
    )
    return (total, summed)


def kv_sum(part, base, kv_slot, n_kv):
    rows = part.shape[0] // n_kv
    got = lax.all_to_all(
        part.astype(jnp.bfloat16).reshape(n_kv, rows, part.shape[1]), "kv", 0, 0, tiled=False
    )
    own = lax.dynamic_slice_in_dim(base, kv_slot * rows, rows, 0)
    chunk = (own + jnp.sum(got.astype(jnp.float32), axis=0)).astype(jnp.bfloat16)
    spread = jnp.broadcast_to(chunk[None], (n_kv,) + chunk.shape)
    return lax.all_to_all(spread, "kv", 0, 0, tiled=False).reshape(part.shape)


def per_device(
    tokens,
    norm_in,
    w_qkv,
    qkv_bias,
    w_out,
    norm_mid,
    w_gate,
    w_up,
    w_down,
    short_keys,
    short_values,
    short_len,
    long_keys,
    long_values,
    long_len,
    positions,
):
    heads_here = short_keys.shape[2]
    scale = HD ** (-0.5)
    wide = tokens.astype(jnp.float32)
    slot = lax.axis_index("req")
    kv_slot = lax.axis_index("kv")
    n_req = tokens.shape[0] // REQ_DEV
    n_kv = lax.psum(1, "kv")
    square_part = jnp.sum(wide * wide, axis=1)
    square_hi = square_part.astype(jnp.bfloat16)
    square_lo = (square_part - square_hi.astype(jnp.float32)).astype(jnp.bfloat16)
    square_cols = jnp.pad(jnp.stack([square_hi, square_lo], axis=1), ((0, 0), (0, 126)))
    gained = (wide * norm_in.astype(jnp.float32)[None, :]).astype(jnp.bfloat16)
    qkv_part = jnp.dot(gained, w_qkv, preferred_element_type=jnp.float32).astype(jnp.bfloat16)
    width = qkv_part.shape[1]
    sent = jnp.concatenate([qkv_part, square_cols], axis=1).reshape(n_req, REQ_DEV, width + 128)
    got = lax.all_to_all(sent, "req", 0, 0, tiled=False).astype(jnp.float32)
    united = jnp.sum(got[:, :, :width], axis=0)
    square_in = jnp.sum(got[:, :, width] + got[:, :, width + 1], axis=0)
    scale_in = lax.rsqrt(square_in / D + EPS)
    united = (united * scale_in[:, None] + qkv_bias.astype(jnp.float32)[None, :]).reshape(
        REQ_DEV, heads_here, GROUP + 2, HD
    )
    inv_freq = THETA ** (-(2.0 * jnp.arange(HD // 2, dtype=jnp.float32)) / HD)
    angles = positions.astype(jnp.float32)[:, None] * inv_freq[None, :]
    queries = rotate(united[:, :, :GROUP], angles[:, None, None, :]).astype(jnp.bfloat16)
    new_keys = rotate(united[:, :, GROUP], angles[:, None, :]).astype(jnp.bfloat16)
    new_values = united[:, :, GROUP + 1].astype(jnp.bfloat16)
    short_raw = (
        jnp.einsum("rhgd,rshd->rhgs", queries, short_keys, preferred_element_type=jnp.float32)
        * scale
    )
    live = jnp.arange(SHORT_CAP)[None, :] < short_len[:, None]
    short_raw = jnp.where(live[:, None, None, :], short_raw, NEGATIVE)
    own_raw = (
        jnp.einsum("rhgd,rhd->rhg", queries, new_keys, preferred_element_type=jnp.float32) * scale
    )
    peak = jnp.maximum(jnp.max(short_raw, axis=3), own_raw)
    slot_len = lax.dynamic_index_in_dim(long_len, slot, 0, keepdims=False)
    long_raw = (
        jnp.einsum("hgd,lhd->hgl", queries[0], long_keys[0], preferred_element_type=jnp.float32)
        * scale
    )
    long_live = jnp.arange(LONG_CAP) < slot_len
    long_raw = jnp.where(long_live[None, None, :], long_raw, NEGATIVE)
    first_peak = jnp.maximum(peak[0], jnp.max(long_raw, axis=2))
    peak = jnp.concatenate([first_peak[None], peak[1:]], axis=0)
    total, summed = weigh(short_raw, own_raw, short_values, new_values, peak)
    long_weights = jnp.where(
        long_live[None, None, :], jnp.exp(long_raw - first_peak[:, :, None]), 0.0
    )
    long_summed = jnp.einsum(
        "hgl,lhd->hgd",
        long_weights.astype(jnp.bfloat16),
        long_values[0],
        preferred_element_type=jnp.float32,
    )
    total = total.at[0].add(jnp.sum(long_weights, axis=2))
    summed = summed.at[0].add(long_summed)
    attended = (
        (summed / total[..., None]).astype(jnp.bfloat16).reshape(REQ_DEV, heads_here * GROUP * HD)
    )
    out_part = jnp.dot(
        lax.all_gather(attended, "req", axis=0, tiled=True),
        w_out,
        preferred_element_type=jnp.float32,
    )
    residual = kv_sum(out_part, wide, kv_slot, n_kv)
    resid_wide = residual.astype(jnp.float32)
    square_mid = lax.psum(jnp.sum(resid_wide * resid_wide, axis=1), "req")
    mixed_in = (resid_wide * norm_mid.astype(jnp.float32)[None, :]).astype(jnp.bfloat16)
    units = w_gate.shape[1]
    padded = -(-units // 128) * 128
    w_gate_up = jnp.concatenate(
        [
            jnp.pad(w_gate, ((0, 0), (0, padded - units))),
            jnp.pad(w_up, ((0, 0), (0, padded - units))),
        ],
        axis=1,
    )
    gate_up = lax.psum_scatter(
        jnp.dot(mixed_in, w_gate_up, preferred_element_type=jnp.float32).astype(jnp.bfloat16),
        "req",
        scatter_dimension=0,
        tiled=True,
    ).astype(jnp.float32)
    scale_mid = lax.rsqrt(lax.dynamic_slice_in_dim(square_mid, slot * REQ_DEV, REQ_DEV) / D + EPS)
    gate = gate_up[:, :units] * scale_mid[:, None]
    up = gate_up[:, padded : padded + units] * scale_mid[:, None]
    act = (jax.nn.silu(gate) * up).astype(jnp.bfloat16)
    down_part = jnp.dot(
        lax.all_gather(act, "req", axis=0, tiled=True), w_down, preferred_element_type=jnp.float32
    )
    return kv_sum(down_part, resid_wide, kv_slot, n_kv)


def solution(mesh):
    placed = (
        P(None, "req"),
        P("req"),
        P("req", "kv"),
        P("kv"),
        P("kv", "req"),
        P("req"),
        P("req", "kv"),
        P("req", "kv"),
        P("kv", "req"),
        P("req", None, "kv", None),
        P("req", None, "kv", None),
        P("req"),
        P("req", None, "kv", None),
        P("req", None, "kv", None),
        P(),
        P("req"),
    )
    return jax.shard_map(
        per_device, mesh=mesh, in_specs=placed, out_specs=P(None, "req"), check_vma=False
    )
```

```python
import jax
import jax.numpy as jnp
from jax import lax
from jax.sharding import PartitionSpec as P

D = 8192
HD = 128
SHORT_CAP = 256
LONG_CAP = 8192
REQ_DEV = 64
GROUP = 8


EPS = 1e-06
THETA = 1000000.0
NEGATIVE = -1e30


def rotate(values, angles):
    half = values.shape[-1] // 2
    first = values[..., :half]
    second = values[..., half:]
    cosine = jnp.cos(angles)
    sine = jnp.sin(angles)
    return jnp.concatenate(
        [first * cosine - second * sine, second * cosine + first * sine], axis=-1
    )


def weigh(short_raw, own_raw, short_values, own_values, peak):
    short_weights = jnp.exp(short_raw - peak[..., None])
    own_weights = jnp.exp(own_raw - peak)
    total = jnp.sum(short_weights, axis=3) + own_weights
    summed = jnp.einsum(
        "rhgs,rshd->rhgd",
        short_weights.astype(jnp.bfloat16),
        short_values,
        preferred_element_type=jnp.float32,
    )
    summed = summed + jnp.einsum(
        "rhg,rhd->rhgd",
        own_weights.astype(jnp.bfloat16),
        own_values,
        preferred_element_type=jnp.float32,
    )
    return (total, summed)


def kv_sum(part, base, kv_slot, n_kv):
    rows = part.shape[0] // n_kv
    got = lax.all_to_all(
        part.astype(jnp.bfloat16).reshape(n_kv, rows, part.shape[1]), "kv", 0, 0, tiled=False
    )
    own = lax.dynamic_slice_in_dim(base, kv_slot * rows, rows, 0)
    chunk = (own + jnp.sum(got.astype(jnp.float32), axis=0)).astype(jnp.bfloat16)
    spread = jnp.broadcast_to(chunk[None], (n_kv,) + chunk.shape)
    return lax.all_to_all(spread, "kv", 0, 0, tiled=False).reshape(part.shape)


def per_device(
    tokens,
    norm_in,
    w_qkv,
    qkv_bias,
    w_out,
    norm_mid,
    w_gate,
    w_up,
    w_down,
    short_keys,
    short_values,
    short_len,
    long_keys,
    long_values,
    long_len,
    positions,
):
    heads_here = short_keys.shape[2]
    scale = HD ** (-0.5)
    wide = tokens.astype(jnp.float32)
    slot = lax.axis_index("req")
    kv_slot = lax.axis_index("kv")
    n_req = tokens.shape[0] // REQ_DEV
    n_kv = lax.psum(1, "kv")
    square_part = jnp.sum(wide * wide, axis=1)
    square_hi = square_part.astype(jnp.bfloat16)
    square_lo = (square_part - square_hi.astype(jnp.float32)).astype(jnp.bfloat16)
    square_cols = jnp.pad(jnp.stack([square_hi, square_lo], axis=1), ((0, 0), (0, 126)))
    gained = (wide * norm_in.astype(jnp.float32)[None, :]).astype(jnp.bfloat16)
    qkv_part = jnp.dot(gained, w_qkv, preferred_element_type=jnp.float32).astype(jnp.bfloat16)
    width = qkv_part.shape[1]
    sent = jnp.concatenate([qkv_part, square_cols], axis=1).reshape(n_req, REQ_DEV, width + 128)
    got = lax.all_to_all(sent, "req", 0, 0, tiled=False).astype(jnp.float32)
    united = jnp.sum(got[:, :, :width], axis=0)
    square_in = jnp.sum(got[:, :, width] + got[:, :, width + 1], axis=0)
    scale_in = lax.rsqrt(square_in / D + EPS)
    united = (united * scale_in[:, None] + qkv_bias.astype(jnp.float32)[None, :]).reshape(
        REQ_DEV, heads_here, GROUP + 2, HD
    )
    inv_freq = THETA ** (-(2.0 * jnp.arange(HD // 2, dtype=jnp.float32)) / HD)
    angles = positions.astype(jnp.float32)[:, None] * inv_freq[None, :]
    queries = rotate(united[:, :, :GROUP], angles[:, None, None, :]).astype(jnp.bfloat16)
    new_keys = rotate(united[:, :, GROUP], angles[:, None, :]).astype(jnp.bfloat16)
    new_values = united[:, :, GROUP + 1].astype(jnp.bfloat16)
    short_raw = (
        jnp.einsum("rhgd,rshd->rhgs", queries, short_keys, preferred_element_type=jnp.float32)
        * scale
    )
    live = jnp.arange(SHORT_CAP)[None, :] < short_len[:, None]
    short_raw = jnp.where(live[:, None, None, :], short_raw, NEGATIVE)
    own_raw = (
        jnp.einsum("rhgd,rhd->rhg", queries, new_keys, preferred_element_type=jnp.float32) * scale
    )
    peak = jnp.maximum(jnp.max(short_raw, axis=3), own_raw)
    slot_len = lax.dynamic_index_in_dim(long_len, slot, 0, keepdims=False)
    long_raw = (
        jnp.einsum("hgd,lhd->hgl", queries[0], long_keys[0], preferred_element_type=jnp.float32)
        * scale
    )
    long_live = jnp.arange(LONG_CAP) < slot_len
    long_raw = jnp.where(long_live[None, None, :], long_raw, NEGATIVE)
    first_peak = jnp.maximum(peak[0], jnp.max(long_raw, axis=2))
    peak = jnp.concatenate([first_peak[None], peak[1:]], axis=0)
    total, summed = weigh(short_raw, own_raw, short_values, new_values, peak)
    long_weights = jnp.where(
        long_live[None, None, :], jnp.exp(long_raw - first_peak[:, :, None]), 0.0
    )
    long_summed = jnp.einsum(
        "hgl,lhd->hgd",
        long_weights.astype(jnp.bfloat16),
        long_values[0],
        preferred_element_type=jnp.float32,
    )
    total = total.at[0].add(jnp.sum(long_weights, axis=2))
    summed = summed.at[0].add(long_summed)
    attended = (
        (summed / total[..., None]).astype(jnp.bfloat16).reshape(REQ_DEV, heads_here * GROUP * HD)
    )
    out_part = jnp.dot(
        lax.all_to_all(
            jnp.broadcast_to(attended[None], (n_req,) + attended.shape), "req", 0, 0, tiled=False
        ).reshape(n_req * REQ_DEV, attended.shape[1]),
        w_out,
        preferred_element_type=jnp.float32,
    )
    residual = kv_sum(out_part, wide, kv_slot, n_kv)
    resid_wide = residual.astype(jnp.float32)
    square_mid = lax.psum(jnp.sum(resid_wide * resid_wide, axis=1), "req")
    mixed_in = (resid_wide * norm_mid.astype(jnp.float32)[None, :]).astype(jnp.bfloat16)
    units = w_gate.shape[1]
    padded = -(-units // 128) * 128
    w_gate_up = jnp.concatenate(
        [
            jnp.pad(w_gate, ((0, 0), (0, padded - units))),
            jnp.pad(w_up, ((0, 0), (0, padded - units))),
        ],
        axis=1,
    )
    gate_up = lax.psum_scatter(
        jnp.dot(mixed_in, w_gate_up, preferred_element_type=jnp.float32).astype(jnp.bfloat16),
        "req",
        scatter_dimension=0,
        tiled=True,
    ).astype(jnp.float32)
    scale_mid = lax.rsqrt(lax.dynamic_slice_in_dim(square_mid, slot * REQ_DEV, REQ_DEV) / D + EPS)
    gate = gate_up[:, :units] * scale_mid[:, None]
    up = gate_up[:, padded : padded + units] * scale_mid[:, None]
    act = (jax.nn.silu(gate) * up).astype(jnp.bfloat16)
    down_part = jnp.dot(
        lax.all_gather(act, "req", axis=0, tiled=True), w_down, preferred_element_type=jnp.float32
    )
    return kv_sum(down_part, resid_wide, kv_slot, n_kv)


def solution(mesh):
    placed = (
        P(None, "req"),
        P("req"),
        P("req", "kv"),
        P("kv"),
        P("kv", "req"),
        P("req"),
        P("req", "kv"),
        P("req", "kv"),
        P("kv", "req"),
        P("req", None, "kv", None),
        P("req", None, "kv", None),
        P("req"),
        P("req", None, "kv", None),
        P("req", None, "kv", None),
        P(),
        P("req"),
    )
    return jax.shard_map(
        per_device, mesh=mesh, in_specs=placed, out_specs=P(None, "req"), check_vma=False
    )
```

```python
import jax
import jax.numpy as jnp
from jax import lax
from jax.sharding import PartitionSpec as P

D = 8192
HD = 128
SHORT_CAP = 256
LONG_CAP = 8192
REQ_DEV = 64
GROUP = 8


EPS = 1e-06
THETA = 1000000.0
NEGATIVE = -1e30


def rotate(values, angles):
    half = values.shape[-1] // 2
    first = values[..., :half]
    second = values[..., half:]
    cosine = jnp.cos(angles)
    sine = jnp.sin(angles)
    return jnp.concatenate(
        [first * cosine - second * sine, second * cosine + first * sine], axis=-1
    )


def weigh(short_raw, own_raw, short_values, own_values, peak):
    short_weights = jnp.exp(short_raw - peak[..., None])
    own_weights = jnp.exp(own_raw - peak)
    total = jnp.sum(short_weights, axis=3) + own_weights
    summed = jnp.einsum(
        "rhgs,rshd->rhgd",
        short_weights.astype(jnp.bfloat16),
        short_values,
        preferred_element_type=jnp.float32,
    )
    summed = summed + jnp.einsum(
        "rhg,rhd->rhgd",
        own_weights.astype(jnp.bfloat16),
        own_values,
        preferred_element_type=jnp.float32,
    )
    return (total, summed)


def kv_sum(part, base, kv_slot, n_kv):
    rows = part.shape[0] // n_kv
    got = lax.all_to_all(
        part.astype(jnp.bfloat16).reshape(n_kv, rows, part.shape[1]), "kv", 0, 0, tiled=False
    )
    own = lax.dynamic_slice_in_dim(base, kv_slot * rows, rows, 0)
    chunk = (own + jnp.sum(got, axis=0, dtype=jnp.float32)).astype(jnp.bfloat16)
    spread = jnp.broadcast_to(chunk[None], (n_kv,) + chunk.shape)
    return lax.all_to_all(spread, "kv", 0, 0, tiled=False).reshape(part.shape)


def per_device(
    tokens,
    norm_in,
    w_qkv,
    qkv_bias,
    w_out,
    norm_mid,
    w_gate,
    w_up,
    w_down,
    short_keys,
    short_values,
    short_len,
    long_keys,
    long_values,
    long_len,
    positions,
):
    heads_here = short_keys.shape[2]
    scale = HD ** (-0.5)
    wide = tokens.astype(jnp.float32)
    slot = lax.axis_index("req")
    kv_slot = lax.axis_index("kv")
    n_req = tokens.shape[0] // REQ_DEV
    n_kv = lax.psum(1, "kv")
    square_part = jnp.sum(wide * wide, axis=1)
    square_hi = square_part.astype(jnp.bfloat16)
    square_lo = (square_part - square_hi.astype(jnp.float32)).astype(jnp.bfloat16)
    square_cols = jnp.pad(jnp.stack([square_hi, square_lo], axis=1), ((0, 0), (0, 126)))
    gained = (wide * norm_in.astype(jnp.float32)[None, :]).astype(jnp.bfloat16)
    qkv_part = jnp.dot(gained, w_qkv, preferred_element_type=jnp.float32).astype(jnp.bfloat16)
    width = qkv_part.shape[1]
    sent = jnp.concatenate([qkv_part, square_cols], axis=1).reshape(n_req, REQ_DEV, width + 128)
    got = lax.all_to_all(sent, "req", 0, 0, tiled=False)
    united = jnp.sum(got[:, :, :width], axis=0, dtype=jnp.float32)
    square_in = jnp.sum(got[:, :, width : width + 2], axis=(0, 2), dtype=jnp.float32)
    scale_in = lax.rsqrt(square_in / D + EPS)
    united = (united * scale_in[:, None] + qkv_bias.astype(jnp.float32)[None, :]).reshape(
        REQ_DEV, heads_here, GROUP + 2, HD
    )
    inv_freq = THETA ** (-(2.0 * jnp.arange(HD // 2, dtype=jnp.float32)) / HD)
    angles = positions.astype(jnp.float32)[:, None] * inv_freq[None, :]
    queries = rotate(united[:, :, :GROUP], angles[:, None, None, :]).astype(jnp.bfloat16)
    new_keys = rotate(united[:, :, GROUP], angles[:, None, :]).astype(jnp.bfloat16)
    new_values = united[:, :, GROUP + 1].astype(jnp.bfloat16)
    short_raw = (
        jnp.einsum("rhgd,rshd->rhgs", queries, short_keys, preferred_element_type=jnp.float32)
        * scale
    )
    live = jnp.arange(SHORT_CAP)[None, :] < short_len[:, None]
    short_raw = jnp.where(live[:, None, None, :], short_raw, NEGATIVE)
    own_raw = (
        jnp.einsum("rhgd,rhd->rhg", queries, new_keys, preferred_element_type=jnp.float32) * scale
    )
    peak = jnp.maximum(jnp.max(short_raw, axis=3), own_raw)
    slot_len = lax.dynamic_index_in_dim(long_len, slot, 0, keepdims=False)
    long_raw = (
        jnp.einsum("hgd,lhd->hgl", queries[0], long_keys[0], preferred_element_type=jnp.float32)
        * scale
    )
    long_live = jnp.arange(LONG_CAP) < slot_len
    long_raw = jnp.where(long_live[None, None, :], long_raw, NEGATIVE)
    first_peak = jnp.maximum(peak[0], jnp.max(long_raw, axis=2))
    peak = jnp.concatenate([first_peak[None], peak[1:]], axis=0)
    total, summed = weigh(short_raw, own_raw, short_values, new_values, peak)
    long_weights = jnp.where(
        long_live[None, None, :], jnp.exp(long_raw - first_peak[:, :, None]), 0.0
    )
    long_summed = jnp.einsum(
        "hgl,lhd->hgd",
        long_weights.astype(jnp.bfloat16),
        long_values[0],
        preferred_element_type=jnp.float32,
    )
    total = total.at[0].add(jnp.sum(long_weights, axis=2))
    summed = summed.at[0].add(long_summed)
    attended = (
        (summed / total[..., None]).astype(jnp.bfloat16).reshape(REQ_DEV, heads_here * GROUP * HD)
    )
    out_part = jnp.dot(
        lax.all_to_all(
            jnp.broadcast_to(attended[None], (n_req,) + attended.shape), "req", 0, 0, tiled=False
        ).reshape(n_req * REQ_DEV, attended.shape[1]),
        w_out,
        preferred_element_type=jnp.float32,
    )
    residual = kv_sum(out_part, wide, kv_slot, n_kv)
    resid_wide = residual.astype(jnp.float32)
    square_mid = lax.psum(jnp.sum(resid_wide * resid_wide, axis=1), "req")
    mixed_in = (resid_wide * norm_mid.astype(jnp.float32)[None, :]).astype(jnp.bfloat16)
    units = w_gate.shape[1]
    padded = -(-units // 128) * 128
    w_gate_up = jnp.concatenate(
        [
            jnp.pad(w_gate, ((0, 0), (0, padded - units))),
            jnp.pad(w_up, ((0, 0), (0, padded - units))),
        ],
        axis=1,
    )
    gate_up = lax.psum_scatter(
        jnp.dot(mixed_in, w_gate_up, preferred_element_type=jnp.float32).astype(jnp.bfloat16),
        "req",
        scatter_dimension=0,
        tiled=True,
    )
    scale_mid = lax.rsqrt(lax.dynamic_slice_in_dim(square_mid, slot * REQ_DEV, REQ_DEV) / D + EPS)
    gate = gate_up[:, :units].astype(jnp.float32) * scale_mid[:, None]
    up = gate_up[:, padded : padded + units].astype(jnp.float32) * scale_mid[:, None]
    act = (jax.nn.silu(gate) * up).astype(jnp.bfloat16)
    down_part = jnp.dot(
        lax.all_gather(act, "req", axis=0, tiled=True), w_down, preferred_element_type=jnp.float32
    )
    return kv_sum(down_part, resid_wide, kv_slot, n_kv)


def solution(mesh):
    placed = (
        P(None, "req"),
        P("req"),
        P("req", "kv"),
        P("kv"),
        P("kv", "req"),
        P("req"),
        P("req", "kv"),
        P("req", "kv"),
        P("kv", "req"),
        P("req", None, "kv", None),
        P("req", None, "kv", None),
        P("req"),
        P("req", None, "kv", None),
        P("req", None, "kv", None),
        P(),
        P("req"),
    )
    return jax.shard_map(
        per_device, mesh=mesh, in_specs=placed, out_specs=P(None, "req"), check_vma=False
    )
```

```python
import jax
import jax.numpy as jnp
from jax import lax
from jax.sharding import PartitionSpec as P

D = 8192
HD = 128
SHORT_CAP = 256
LONG_CAP = 8192
REQ_DEV = 64
GROUP = 8


EPS = 1e-06
THETA = 1000000.0
NEGATIVE = -1e30


def rotate(values, angles):
    half = values.shape[-1] // 2
    first = values[..., :half]
    second = values[..., half:]
    cosine = jnp.cos(angles)
    sine = jnp.sin(angles)
    return jnp.concatenate(
        [first * cosine - second * sine, second * cosine + first * sine], axis=-1
    )


def weigh(short_raw, own_raw, short_values, own_values, peak):
    short_weights = jnp.exp(short_raw - peak[..., None])
    own_weights = jnp.exp(own_raw - peak)
    total = jnp.sum(short_weights, axis=3) + own_weights
    summed = jnp.einsum(
        "rhgs,rshd->rhgd",
        short_weights.astype(jnp.bfloat16),
        short_values,
        preferred_element_type=jnp.float32,
    )
    summed = summed + jnp.einsum(
        "rhg,rhd->rhgd",
        own_weights.astype(jnp.bfloat16),
        own_values,
        preferred_element_type=jnp.float32,
    )
    return (total, summed)


def kv_sum(part, base, kv_slot, n_kv):
    rows = part.shape[0] // n_kv
    got = lax.all_to_all(
        part.astype(jnp.bfloat16).reshape(n_kv, rows, part.shape[1]), "kv", 0, 0, tiled=False
    )
    own = lax.dynamic_slice_in_dim(base, kv_slot * rows, rows, 0)
    chunk = (own + jnp.sum(got.astype(jnp.float32), axis=0)).astype(jnp.bfloat16)
    spread = jnp.broadcast_to(chunk[None], (n_kv,) + chunk.shape)
    return lax.all_to_all(spread, "kv", 0, 0, tiled=False).reshape(part.shape)


def per_device(
    tokens,
    norm_in,
    w_qkv,
    qkv_bias,
    w_out,
    norm_mid,
    w_gate,
    w_up,
    w_down,
    short_keys,
    short_values,
    short_len,
    long_keys,
    long_values,
    long_len,
    positions,
):
    heads_here = short_keys.shape[2]
    scale = HD ** (-0.5)
    wide = tokens.astype(jnp.float32)
    slot = lax.axis_index("req")
    kv_slot = lax.axis_index("kv")
    n_req = tokens.shape[0] // REQ_DEV
    n_kv = lax.psum(1, "kv")
    square_in = lax.psum(jnp.sum(wide * wide, axis=1), "req")
    gained = (wide * norm_in.astype(jnp.float32)[None, :]).astype(jnp.bfloat16)
    qkv_part = jnp.dot(gained, w_qkv, preferred_element_type=jnp.float32).astype(jnp.bfloat16)
    width = qkv_part.shape[1]
    got = lax.all_to_all(qkv_part.reshape(n_req, REQ_DEV, width), "req", 0, 0, tiled=False)
    united = jnp.sum(got.astype(jnp.float32), axis=0)
    square_in = lax.dynamic_slice_in_dim(square_in, slot * REQ_DEV, REQ_DEV)
    scale_in = lax.rsqrt(square_in / D + EPS)
    united = (united * scale_in[:, None] + qkv_bias.astype(jnp.float32)[None, :]).reshape(
        REQ_DEV, heads_here, GROUP + 2, HD
    )
    inv_freq = THETA ** (-(2.0 * jnp.arange(HD // 2, dtype=jnp.float32)) / HD)
    angles = positions.astype(jnp.float32)[:, None] * inv_freq[None, :]
    queries = rotate(united[:, :, :GROUP], angles[:, None, None, :]).astype(jnp.bfloat16)
    new_keys = rotate(united[:, :, GROUP], angles[:, None, :]).astype(jnp.bfloat16)
    new_values = united[:, :, GROUP + 1].astype(jnp.bfloat16)
    short_raw = (
        jnp.einsum("rhgd,rshd->rhgs", queries, short_keys, preferred_element_type=jnp.float32)
        * scale
    )
    live = jnp.arange(SHORT_CAP)[None, :] < short_len[:, None]
    short_raw = jnp.where(live[:, None, None, :], short_raw, NEGATIVE)
    own_raw = (
        jnp.einsum("rhgd,rhd->rhg", queries, new_keys, preferred_element_type=jnp.float32) * scale
    )
    peak = jnp.maximum(jnp.max(short_raw, axis=3), own_raw)
    slot_len = lax.dynamic_index_in_dim(long_len, slot, 0, keepdims=False)
    long_raw = (
        jnp.einsum("hgd,lhd->hgl", queries[0], long_keys[0], preferred_element_type=jnp.float32)
        * scale
    )
    long_live = jnp.arange(LONG_CAP) < slot_len
    long_raw = jnp.where(long_live[None, None, :], long_raw, NEGATIVE)
    first_peak = jnp.maximum(peak[0], jnp.max(long_raw, axis=2))
    peak = jnp.concatenate([first_peak[None], peak[1:]], axis=0)
    total, summed = weigh(short_raw, own_raw, short_values, new_values, peak)
    long_weights = jnp.where(
        long_live[None, None, :], jnp.exp(long_raw - first_peak[:, :, None]), 0.0
    )
    long_summed = jnp.einsum(
        "hgl,lhd->hgd",
        long_weights.astype(jnp.bfloat16),
        long_values[0],
        preferred_element_type=jnp.float32,
    )
    total = total.at[0].add(jnp.sum(long_weights, axis=2))
    summed = summed.at[0].add(long_summed)
    attended = (
        (summed / total[..., None]).astype(jnp.bfloat16).reshape(REQ_DEV, heads_here * GROUP * HD)
    )
    out_part = jnp.dot(
        lax.all_to_all(
            jnp.broadcast_to(attended[None], (n_req,) + attended.shape), "req", 0, 0, tiled=False
        ).reshape(n_req * REQ_DEV, attended.shape[1]),
        w_out,
        preferred_element_type=jnp.float32,
    )
    residual = kv_sum(out_part, wide, kv_slot, n_kv)
    resid_wide = residual.astype(jnp.float32)
    square_mid = lax.psum(jnp.sum(resid_wide * resid_wide, axis=1), "req")
    mixed_in = (resid_wide * norm_mid.astype(jnp.float32)[None, :]).astype(jnp.bfloat16)
    units = w_gate.shape[1]
    padded = -(-units // 128) * 128
    w_gate_up = jnp.concatenate(
        [
            jnp.pad(w_gate, ((0, 0), (0, padded - units))),
            jnp.pad(w_up, ((0, 0), (0, padded - units))),
        ],
        axis=1,
    )
    gate_up = lax.psum_scatter(
        jnp.dot(mixed_in, w_gate_up, preferred_element_type=jnp.float32).astype(jnp.bfloat16),
        "req",
        scatter_dimension=0,
        tiled=True,
    ).astype(jnp.float32)
    scale_mid = lax.rsqrt(lax.dynamic_slice_in_dim(square_mid, slot * REQ_DEV, REQ_DEV) / D + EPS)
    gate = gate_up[:, :units] * scale_mid[:, None]
    up = gate_up[:, padded : padded + units] * scale_mid[:, None]
    act = (jax.nn.silu(gate) * up).astype(jnp.bfloat16)
    down_part = jnp.dot(
        lax.all_gather(act, "req", axis=0, tiled=True), w_down, preferred_element_type=jnp.float32
    )
    return kv_sum(down_part, resid_wide, kv_slot, n_kv)


def solution(mesh):
    placed = (
        P(None, "req"),
        P("req"),
        P("req", "kv"),
        P("kv"),
        P("kv", "req"),
        P("req"),
        P("req", "kv"),
        P("req", "kv"),
        P("kv", "req"),
        P("req", None, "kv", None),
        P("req", None, "kv", None),
        P("req"),
        P("req", None, "kv", None),
        P("req", None, "kv", None),
        P(),
        P("req"),
    )
    return jax.shard_map(
        per_device, mesh=mesh, in_specs=placed, out_specs=P(None, "req"), check_vma=False
    )
```

```python
import jax
import jax.numpy as jnp
from jax import lax
from jax.sharding import PartitionSpec as P

D = 8192
HD = 128
SHORT_CAP = 256
LONG_CAP = 8192
REQ_DEV = 64
GROUP = 8


EPS = 1e-06
THETA = 1000000.0
NEGATIVE = -1e30


def rotate(values, angles):
    half = values.shape[-1] // 2
    first = values[..., :half]
    second = values[..., half:]
    cosine = jnp.cos(angles)
    sine = jnp.sin(angles)
    return jnp.concatenate(
        [first * cosine - second * sine, second * cosine + first * sine], axis=-1
    )


def weigh(short_raw, own_raw, short_values, own_values, peak):
    short_weights = jnp.exp(short_raw - peak[..., None])
    own_weights = jnp.exp(own_raw - peak)
    total = jnp.sum(short_weights, axis=3) + own_weights
    summed = jnp.einsum(
        "rhgs,rshd->rhgd",
        short_weights.astype(jnp.bfloat16),
        short_values,
        preferred_element_type=jnp.float32,
    )
    summed = summed + jnp.einsum(
        "rhg,rhd->rhgd",
        own_weights.astype(jnp.bfloat16),
        own_values,
        preferred_element_type=jnp.float32,
    )
    return (total, summed)


def kv_sum(part, base, kv_slot, n_kv):
    rows = part.shape[0] // n_kv
    got = lax.all_to_all(
        part.astype(jnp.bfloat16).reshape(n_kv, rows, part.shape[1]), "kv", 0, 0, tiled=False
    )
    own = lax.dynamic_slice_in_dim(base, kv_slot * rows, rows, 0)
    chunk = (own + jnp.sum(got.astype(jnp.float32), axis=0)).astype(jnp.bfloat16)
    spread = jnp.broadcast_to(chunk[None], (n_kv,) + chunk.shape)
    return lax.all_to_all(spread, "kv", 0, 0, tiled=False).reshape(part.shape)


def per_device(
    tokens,
    norm_in,
    w_qkv,
    qkv_bias,
    w_out,
    norm_mid,
    w_gate,
    w_up,
    w_down,
    short_keys,
    short_values,
    short_len,
    long_keys,
    long_values,
    long_len,
    positions,
):
    heads_here = short_keys.shape[2]
    scale = HD ** (-0.5)
    wide = tokens.astype(jnp.float32)
    slot = lax.axis_index("req")
    kv_slot = lax.axis_index("kv")
    n_req = tokens.shape[0] // REQ_DEV
    n_kv = lax.psum(1, "kv")
    square_part = jnp.sum(wide * wide, axis=1)
    square_hi = square_part.astype(jnp.bfloat16)
    square_lo = (square_part - square_hi.astype(jnp.float32)).astype(jnp.bfloat16)
    square_cols = jnp.pad(jnp.stack([square_hi, square_lo], axis=1), ((0, 0), (0, 126)))
    gained = (wide * norm_in.astype(jnp.float32)[None, :]).astype(jnp.bfloat16)
    qkv_part = jnp.dot(gained, w_qkv, preferred_element_type=jnp.float32).astype(jnp.bfloat16)
    width = qkv_part.shape[1]
    sent = jnp.concatenate([qkv_part, square_cols], axis=1).reshape(n_req, REQ_DEV, width + 128)
    got = lax.all_to_all(sent, "req", 0, 0, tiled=False).astype(jnp.float32)
    united = jnp.sum(got[:, :, :width], axis=0)
    square_in = jnp.sum(got[:, :, width] + got[:, :, width + 1], axis=0)
    scale_in = lax.rsqrt(square_in / D + EPS)
    united = (united * scale_in[:, None] + qkv_bias.astype(jnp.float32)[None, :]).reshape(
        REQ_DEV, heads_here, GROUP + 2, HD
    )
    inv_freq = THETA ** (-(2.0 * jnp.arange(HD // 2, dtype=jnp.float32)) / HD)
    angles = positions.astype(jnp.float32)[:, None] * inv_freq[None, :]
    queries = rotate(united[:, :, :GROUP], angles[:, None, None, :]).astype(jnp.bfloat16)
    new_keys = rotate(united[:, :, GROUP], angles[:, None, :]).astype(jnp.bfloat16)
    new_values = united[:, :, GROUP + 1].astype(jnp.bfloat16)
    short_raw = (
        jnp.einsum("rhgd,rshd->rhgs", queries, short_keys, preferred_element_type=jnp.float32)
        * scale
    )
    live = jnp.arange(SHORT_CAP)[None, :] < short_len[:, None]
    short_raw = jnp.where(live[:, None, None, :], short_raw, NEGATIVE)
    own_raw = (
        jnp.einsum("rhgd,rhd->rhg", queries, new_keys, preferred_element_type=jnp.float32) * scale
    )
    peak = jnp.maximum(jnp.max(short_raw, axis=3), own_raw)
    slot_len = lax.dynamic_index_in_dim(long_len, slot, 0, keepdims=False)
    long_raw = (
        jnp.einsum("hgd,lhd->hgl", queries[0], long_keys[0], preferred_element_type=jnp.float32)
        * scale
    )
    long_live = jnp.arange(LONG_CAP) < slot_len
    long_raw = jnp.where(long_live[None, None, :], long_raw, NEGATIVE)
    first_peak = jnp.maximum(peak[0], jnp.max(long_raw, axis=2))
    peak = jnp.concatenate([first_peak[None], peak[1:]], axis=0)
    total, summed = weigh(short_raw, own_raw, short_values, new_values, peak)
    long_weights = jnp.where(
        long_live[None, None, :], jnp.exp(long_raw - first_peak[:, :, None]), 0.0
    )
    long_summed = jnp.einsum(
        "hgl,lhd->hgd",
        long_weights.astype(jnp.bfloat16),
        long_values[0],
        preferred_element_type=jnp.float32,
    )
    total = total.at[0].add(jnp.sum(long_weights, axis=2))
    summed = summed.at[0].add(long_summed)
    attended = (
        (summed / total[..., None]).astype(jnp.bfloat16).reshape(REQ_DEV, heads_here * GROUP * HD)
    )
    out_part = jnp.dot(
        lax.all_to_all(
            jnp.broadcast_to(attended[None], (n_req,) + attended.shape), "req", 0, 0, tiled=False
        ).reshape(n_req * REQ_DEV, attended.shape[1]),
        w_out,
        preferred_element_type=jnp.float32,
    )
    residual = kv_sum(out_part, wide, kv_slot, n_kv)
    resid_wide = residual.astype(jnp.float32)
    square_mid = lax.psum(jnp.sum(resid_wide * resid_wide, axis=1), "req")
    mixed_in = (resid_wide * norm_mid.astype(jnp.float32)[None, :]).astype(jnp.bfloat16)
    units = w_gate.shape[1]
    padded = -(-units // 128) * 128
    w_gate_up = lax.optimization_barrier(
        jnp.concatenate(
            [
                jnp.pad(w_gate, ((0, 0), (0, padded - units))),
                jnp.pad(w_up, ((0, 0), (0, padded - units))),
            ],
            axis=1,
        )
    )
    gate_up = lax.psum_scatter(
        jnp.dot(mixed_in, w_gate_up, preferred_element_type=jnp.float32).astype(jnp.bfloat16),
        "req",
        scatter_dimension=0,
        tiled=True,
    ).astype(jnp.float32)
    scale_mid = lax.rsqrt(lax.dynamic_slice_in_dim(square_mid, slot * REQ_DEV, REQ_DEV) / D + EPS)
    gate = gate_up[:, :units] * scale_mid[:, None]
    up = gate_up[:, padded : padded + units] * scale_mid[:, None]
    act = (jax.nn.silu(gate) * up).astype(jnp.bfloat16)
    down_part = jnp.dot(
        lax.all_gather(act, "req", axis=0, tiled=True), w_down, preferred_element_type=jnp.float32
    )
    return kv_sum(down_part, resid_wide, kv_slot, n_kv)


def solution(mesh):
    placed = (
        P(None, "req"),
        P("req"),
        P("req", "kv"),
        P("kv"),
        P("kv", "req"),
        P("req"),
        P("req", "kv"),
        P("req", "kv"),
        P("kv", "req"),
        P("req", None, "kv", None),
        P("req", None, "kv", None),
        P("req"),
        P("req", None, "kv", None),
        P("req", None, "kv", None),
        P(),
        P("req"),
    )
    return jax.shard_map(
        per_device, mesh=mesh, in_specs=placed, out_specs=P(None, "req"), check_vma=False
    )
```

```python
import jax
import jax.numpy as jnp
from jax import lax
from jax.sharding import PartitionSpec as P

D = 8192
HD = 128
SHORT_CAP = 256
LONG_CAP = 8192
REQ_DEV = 64
GROUP = 8


EPS = 1e-06
THETA = 1000000.0
NEGATIVE = -1e30


def rotate(values, angles):
    half = values.shape[-1] // 2
    first = values[..., :half]
    second = values[..., half:]
    cosine = jnp.cos(angles)
    sine = jnp.sin(angles)
    return jnp.concatenate(
        [first * cosine - second * sine, second * cosine + first * sine], axis=-1
    )


def weigh(short_raw, own_raw, short_values, own_values, peak):
    short_weights = jnp.exp(short_raw - peak[..., None])
    own_weights = jnp.exp(own_raw - peak)
    total = jnp.sum(short_weights, axis=3) + own_weights
    summed = jnp.einsum(
        "rhgs,rshd->rhgd",
        short_weights.astype(jnp.bfloat16),
        short_values,
        preferred_element_type=jnp.float32,
    )
    summed = summed + jnp.einsum(
        "rhg,rhd->rhgd",
        own_weights.astype(jnp.bfloat16),
        own_values,
        preferred_element_type=jnp.float32,
    )
    return (total, summed)


def kv_sum(part, base, kv_slot, n_kv):
    rows = part.shape[0] // n_kv
    got = lax.all_to_all(
        part.astype(jnp.bfloat16).reshape(n_kv, rows, part.shape[1]), "kv", 0, 0, tiled=False
    )
    own = lax.dynamic_slice_in_dim(base, kv_slot * rows, rows, 0)
    chunk = (own + jnp.sum(got.astype(jnp.float32), axis=0)).astype(jnp.bfloat16)
    spread = jnp.broadcast_to(chunk[None], (n_kv,) + chunk.shape)
    return lax.all_to_all(spread, "kv", 0, 0, tiled=False).reshape(part.shape)


def per_device(
    tokens,
    norm_in,
    w_qkv,
    qkv_bias,
    w_out,
    norm_mid,
    w_gate,
    w_up,
    w_down,
    short_keys,
    short_values,
    short_len,
    long_keys,
    long_values,
    long_len,
    positions,
):
    heads_here = short_keys.shape[2]
    scale = HD ** (-0.5)
    wide = tokens.astype(jnp.float32)
    slot = lax.axis_index("req")
    kv_slot = lax.axis_index("kv")
    n_req = tokens.shape[0] // REQ_DEV
    n_kv = lax.psum(1, "kv")
    square_part = jnp.sum(wide * wide, axis=1)
    square_hi = square_part.astype(jnp.bfloat16)
    square_lo = (square_part - square_hi.astype(jnp.float32)).astype(jnp.bfloat16)
    square_cols = jnp.pad(jnp.stack([square_hi, square_lo], axis=1), ((0, 0), (0, 126)))
    gained = (wide * norm_in.astype(jnp.float32)[None, :]).astype(jnp.bfloat16)
    qkv_part = jnp.dot(gained, w_qkv, preferred_element_type=jnp.float32).astype(jnp.bfloat16)
    width = qkv_part.shape[1]
    sent = jnp.concatenate([qkv_part, square_cols], axis=1).reshape(n_req, REQ_DEV, width + 128)
    got = lax.all_to_all(sent, "req", 0, 0, tiled=False).astype(jnp.float32)
    united = jnp.sum(got[:, :, :width], axis=0)
    square_in = jnp.sum(got[:, :, width] + got[:, :, width + 1], axis=0)
    scale_in = lax.rsqrt(square_in / D + EPS)
    united = (united * scale_in[:, None] + qkv_bias.astype(jnp.float32)[None, :]).reshape(
        REQ_DEV, heads_here, GROUP + 2, HD
    )
    inv_freq = THETA ** (-(2.0 * jnp.arange(HD // 2, dtype=jnp.float32)) / HD)
    angles = positions.astype(jnp.float32)[:, None] * inv_freq[None, :]
    queries = rotate(united[:, :, :GROUP], angles[:, None, None, :]).astype(jnp.bfloat16)
    new_keys = rotate(united[:, :, GROUP], angles[:, None, :]).astype(jnp.bfloat16)
    new_values = united[:, :, GROUP + 1].astype(jnp.bfloat16)
    short_raw = (
        jnp.einsum("rhgd,rshd->rhgs", queries, short_keys, preferred_element_type=jnp.float32)
        * scale
    )
    live = jnp.arange(SHORT_CAP)[None, :] < short_len[:, None]
    short_raw = jnp.where(live[:, None, None, :], short_raw, NEGATIVE)
    own_raw = (
        jnp.einsum("rhgd,rhd->rhg", queries, new_keys, preferred_element_type=jnp.float32) * scale
    )
    peak = jnp.maximum(jnp.max(short_raw, axis=3), own_raw)
    slot_len = lax.dynamic_index_in_dim(long_len, slot, 0, keepdims=False)
    long_raw = (
        jnp.einsum("hgd,lhd->hgl", queries[0], long_keys[0], preferred_element_type=jnp.float32)
        * scale
    )
    long_live = jnp.arange(LONG_CAP) < slot_len
    long_raw = jnp.where(long_live[None, None, :], long_raw, NEGATIVE)
    first_peak = jnp.maximum(peak[0], jnp.max(long_raw, axis=2))
    peak = jnp.concatenate([first_peak[None], peak[1:]], axis=0)
    total, summed = weigh(short_raw, own_raw, short_values, new_values, peak)
    long_weights = jnp.where(
        long_live[None, None, :], jnp.exp(long_raw - first_peak[:, :, None]), 0.0
    )
    long_summed = jnp.einsum(
        "hgl,lhd->hgd",
        long_weights.astype(jnp.bfloat16),
        long_values[0],
        preferred_element_type=jnp.float32,
    )
    total = total.at[0].add(jnp.sum(long_weights, axis=2))
    summed = summed.at[0].add(long_summed)
    attended = (
        (summed / total[..., None]).astype(jnp.bfloat16).reshape(REQ_DEV, heads_here * GROUP * HD)
    )
    out_part = jnp.dot(
        lax.all_to_all(
            jnp.broadcast_to(attended[None], (n_req,) + attended.shape), "req", 0, 0, tiled=False
        ).reshape(n_req * REQ_DEV, attended.shape[1]),
        w_out,
        preferred_element_type=jnp.float32,
    )
    residual = kv_sum(out_part, wide, kv_slot, n_kv)
    resid_wide = residual.astype(jnp.float32)
    square_mid = lax.psum(jnp.sum(resid_wide * resid_wide, axis=1), "req")
    mixed_in = (resid_wide * norm_mid.astype(jnp.float32)[None, :]).astype(jnp.bfloat16)
    units = w_gate.shape[1]
    padded = -(-units // 128) * 128
    w_gate_up = lax.optimization_barrier(
        jnp.concatenate(
            [
                jnp.pad(w_gate, ((0, 0), (0, padded - units))),
                jnp.pad(w_up, ((0, 0), (0, padded - units))),
            ],
            axis=1,
        )
    )
    gate_up = lax.psum_scatter(
        jnp.dot(mixed_in, w_gate_up, preferred_element_type=jnp.float32).astype(jnp.bfloat16),
        "req",
        scatter_dimension=0,
        tiled=True,
    ).astype(jnp.float32)
    scale_mid = lax.rsqrt(lax.dynamic_slice_in_dim(square_mid, slot * REQ_DEV, REQ_DEV) / D + EPS)
    gate = gate_up[:, :units] * scale_mid[:, None]
    up = gate_up[:, padded : padded + units] * scale_mid[:, None]
    act = (jax.nn.silu(gate) * up).astype(jnp.bfloat16)
    act = jnp.pad(act, ((0, 0), (0, padded - units)))
    down_part = jnp.dot(
        lax.all_gather(act, "req", axis=0, tiled=True),
        jnp.pad(w_down, ((0, padded - units), (0, 0))),
        preferred_element_type=jnp.float32,
    )
    return kv_sum(down_part, resid_wide, kv_slot, n_kv)


def solution(mesh):
    placed = (
        P(None, "req"),
        P("req"),
        P("req", "kv"),
        P("kv"),
        P("kv", "req"),
        P("req"),
        P("req", "kv"),
        P("req", "kv"),
        P("kv", "req"),
        P("req", None, "kv", None),
        P("req", None, "kv", None),
        P("req"),
        P("req", None, "kv", None),
        P("req", None, "kv", None),
        P(),
        P("req"),
    )
    return jax.shard_map(
        per_device, mesh=mesh, in_specs=placed, out_specs=P(None, "req"), check_vma=False
    )
```
